32 devices in a mesh: expert: 4 (over x, core), hidden: 8 (over z, y).
Axes of the slice: x: 2, y: 2, z: 4, core: 2. Of those that a mesh axis runs over, the one named last changes fastest.
Arguments:
- tokens: bfloat16 [128, 4096], P('hidden', 'expert'), may hold values from -6 to 6
- expert_ids: int32 [128, 2], P('hidden'), may hold values from 0 to 3, all different within a row; in each aligned block of 16 rows (0 to 15, 16 to 31, ...) at most 16 rows name the same one
- gate_vals: float32 [128, 2], P('hidden'), may hold values from 0.2 to 1
- w_gate: bfloat16 [4, 4096, 8192], P('expert', None, 'hidden'), may hold values from -0.09375 to 0.09375
- w_up: bfloat16 [4, 4096, 8192], P('expert', None, 'hidden'), may hold values from -0.09375 to 0.09375
- w_down: bfloat16 [4, 8192, 4096], P('expert', 'hidden'), may hold values from -0.0625 to 0.0625
Outputs:
- mixed: bfloat16 [128, 4096], P('hidden', 'expert')
The draws below stay inside these ranges and needn't reach their ends.
Inputs may be any that keep to these rules, and one draw needn't show every extreme that they name: `expert_ids`: in each aligned block of 16 rows (the tokens of one index of hidden) no expert is named by more than 16 rows, a bound that some block reaches.
All inputs are finite; a program needn't handle non-finite values.
Results may differ from the reference program's by a relative error of at most 0.005.
Values may be sent and summed in bfloat16 or wider, within the bound.
No kernel may reach another device: no remote copies, remote signals or barrier semaphores. Data moves between devices by JAX's collectives and lax.ppermute only.
A program may use at most 128 MiB of HBM per device.

```python
import math
import jax
import jax.numpy as jnp
import numpy as np
from jax import lax

D = 4096
FF = 8192
TOPK = 2
TOK_DEV = 16
EXPERTS = 4
TOKENS = 128
CAP = 16
ROWS = 128


def shard_levels(key, extent, cuts, smallest, high):
    def one(dim, shards_of):
        draws = jax.random.uniform(jax.random.fold_in(jax.random.fold_in(key, 6), dim), (shards_of,), jnp.float32, smallest / len(cuts), high / len(cuts))
        return jnp.repeat(jnp.exp(draws), extent[dim] // shards_of).reshape((-1,) + (1,) * (len(extent) - dim - 1))

    loudness = one(*cuts[0])
    for cut in cuts[1:]:
        loudness = loudness * one(*cut)
    return loudness


def routed_block(rng, own, number, rows, number_of, top, most, lean):
    ranking = jax.random.permutation(rng, number_of)
    packed, common = load_shares(number_of, rows * top, most, lean, True), load_shares(number_of, rows * top, most, lean, False)
    places = jnp.arange(number_of)

    def named(sizes, rotation):
        used = int((sizes > 0).sum())
        fixed = max(1, used // 4)
        moved = fixed + (places - fixed + rotation * (used - fixed)) % max(1, number_of - fixed)
        return jnp.zeros((number_of,), jnp.int32).at[ranking[jnp.where(places < fixed, places, moved)]].set(jnp.asarray(sizes, jnp.int32))

    sizes = jnp.where(number % 4 == 0, named(packed, number // 4), named(common, number - number // 4 - 1))
    mixed = jax.random.permutation(jax.random.fold_in(own, 3), number_of)
    source_of, taker = mixed[0:number_of // 2 * 2:2], mixed[1:number_of // 2 * 2:2]
    room = jnp.minimum(sizes[source_of] - 1, most - sizes[taker]) // 2
    room = jnp.where((source_of == ranking[0]) | (taker == ranking[0]) | (sizes[taker] == 0), 0, jnp.maximum(room, 0))
    moved = jax.random.randint(jax.random.fold_in(own, 4), (number_of // 2,), 0, 1 << 20) % (room + 1)
    sizes = sizes.at[source_of].add(-moved).at[taker].add(moved)
    members = jnp.searchsorted(jnp.cumsum(sizes), jnp.arange(rows * top), side="right").astype(jnp.int32)
    grid = members.reshape(top, rows).T
    grid = grid[jax.random.permutation(jax.random.fold_in(own, 1), rows)]
    rotation = jax.random.randint(jax.random.fold_in(own, 2), (rows, 1), 0, top)
    return jnp.take_along_axis(grid, (jnp.arange(top)[None, :] + rotation) % top, axis=1)


def load_shares(number_of, total, bound, slope, full):
    loads = [(1 << 20) // math.isqrt(rank ** slope) + 1 for rank in range(1, number_of + 1)]
    largest = bound if full else min(bound, max(-(-total // number_of), total * loads[0] // sum(loads)))
    least = 1 if total - largest >= number_of - 1 else 0
    holding, spare = [largest] + [least] * (number_of - 1), total - largest - least * (number_of - 1)
    while spare > 0:
        free = [i for i in range(1, number_of) if holding[i] < largest] or [i for i in range(1, number_of) if holding[i] < bound]
        pool, remaining = sum([loads[i] for i in free]), spare
        for i in free:
            more = min(bound - holding[i], max(1, remaining * loads[i] // pool), spare)
            holding[i] = holding[i] + more
            spare = spare - more
    return np.array(holding)


def bell_draw(own_key, shape, scale, bound, split=(), kind=jnp.bfloat16):
    drawn = scale * jax.random.normal(own_key, shape, jnp.float32)
    if split:
        drawn = drawn * shard_levels(own_key, shape, split, -0.22, 0.18)
    return jnp.clip(drawn, -bound, bound).astype(kind)


def setup_inputs(seed: int = 0) -> dict:
    arg_keys = jax.random.split(jax.random.key(seed), 7)
    tokens = bell_draw(arg_keys[0], (TOKENS, D), 1.0, 6.0, ((0, 8), (1, 4)))
    expert_ids_keys = jax.random.split(jax.random.fold_in(arg_keys[1], 1), TOKENS // TOK_DEV)
    expert_ids_turns = jax.random.permutation(jax.random.fold_in(arg_keys[1], 3), TOKENS // TOK_DEV)
    expert_ids = jax.vmap(lambda own, number: routed_block(jax.random.fold_in(arg_keys[1], 2), own, number, TOK_DEV, EXPERTS, TOPK, CAP, 2))(expert_ids_keys, expert_ids_turns).reshape((TOKENS, TOPK))
    gate_vals = jnp.clip(0.2 + 0.8 * jax.random.uniform(arg_keys[2], (TOKENS, TOPK), jnp.float32) ** shard_levels(arg_keys[2], (TOKENS, TOPK), ((0, 8),), -0.2, 0.2), 0.2, 1.0)
    w_gate = bell_draw(arg_keys[3], (EXPERTS, D, FF), D ** -0.5, 0.09375, ((0, 4), (2, 8)))
    w_up = bell_draw(arg_keys[4], (EXPERTS, D, FF), D ** -0.5, 0.09375, ((0, 4), (2, 8)))
    w_down = bell_draw(arg_keys[5], (EXPERTS, FF, D), FF ** -0.5, 0.0625, ((0, 4), (1, 8)))
    return dict(tokens=tokens, expert_ids=expert_ids, gate_vals=gate_vals, w_gate=w_gate, w_up=w_up, w_down=w_down)


def reference(tokens, expert_ids, gate_vals, w_gate, w_up, w_down):
    flat_ids = expert_ids.reshape(-1)
    gate_flat = gate_vals.reshape(-1)

    def per_expert(expert):
        chosen = flat_ids == expert
        positions = jnp.nonzero(chosen, size=ROWS, fill_value=0)[0]
        is_valid = jnp.arange(ROWS) < jnp.sum(chosen.astype(jnp.int32))
        token_rows = positions // TOPK
        picked = tokens[token_rows]
        gate_part = jnp.dot(picked, w_gate[expert], preferred_element_type=jnp.float32)
        up_part = jnp.dot(picked, w_up[expert], preferred_element_type=jnp.float32)
        hidden = (jax.nn.silu(gate_part) * up_part).astype(jnp.bfloat16)
        expert_out = jnp.dot(hidden, w_down[expert], preferred_element_type=jnp.float32)
        weighting = jnp.where(is_valid, gate_flat[positions], jnp.zeros_like(gate_flat[positions]))
        return expert_out * weighting[:, None], token_rows

    weighted, token_rows = lax.map(per_expert, jnp.arange(EXPERTS))
    mixed_sum = jnp.zeros((TOKENS, D), jnp.float32).at[token_rows.reshape(-1)].add(weighted.reshape(-1, D))
    return mixed_sum.astype(jnp.bfloat16)
```

```python
import jax
import jax.numpy as jnp
from jax import lax
from jax.sharding import PartitionSpec as P


def per_device(tokens, expert_ids, gate_vals, w_gate, w_up, w_down):
    hid = lax.axis_size("hidden")
    exp = lax.axis_size("expert")
    tok_rows, feat = tokens.shape
    groups = hid * exp
    spread = jnp.broadcast_to(tokens[None], (groups, tok_rows, feat))
    pieces = lax.all_to_all(spread, ("hidden", "expert"), 0, 0, tiled=True)
    every_token = (
        pieces.reshape(hid, exp, tok_rows, feat)
        .transpose(0, 2, 1, 3)
        .reshape(hid * tok_rows, exp * feat)
    )
    gate_part = jnp.dot(every_token, w_gate[0], preferred_element_type=jnp.float32)
    up_part = jnp.dot(every_token, w_up[0], preferred_element_type=jnp.float32)
    hidden = (jax.nn.silu(gate_part) * up_part).astype(jnp.bfloat16)
    partial = jnp.dot(hidden, w_down[0], preferred_element_type=jnp.float32)
    outgoing = (
        partial.astype(jnp.bfloat16)
        .reshape(hid, tok_rows, exp, feat)
        .transpose(0, 2, 1, 3)
        .reshape(groups, tok_rows, feat)
    )
    incoming = lax.all_to_all(outgoing, ("hidden", "expert"), 0, 0, tiled=True)
    incoming = incoming.reshape(hid, exp, tok_rows, feat).astype(jnp.float32)
    chosen = expert_ids[:, :, None] == jnp.arange(exp, dtype=expert_ids.dtype)[None, None, :]
    weight = jnp.sum(jnp.where(chosen, gate_vals[:, :, None], 0.0), axis=1)
    per_expert = jnp.sum(incoming, axis=0)
    mixed = jnp.sum(per_expert * weight.T[:, :, None], axis=0)
    return mixed.astype(jnp.bfloat16)


def solution(mesh):
    placed = (
        P("hidden", "expert"),
        P("hidden", None),
        P("hidden", None),
        P("expert", None, "hidden"),
        P("expert", None, "hidden"),
        P("expert", "hidden", None),
    )
    return jax.shard_map(
        per_device, mesh=mesh, in_specs=placed, out_specs=P("hidden", "expert"), check_vma=False
    )
```

```python
import jax
import jax.numpy as jnp
from jax import lax
from jax.sharding import PartitionSpec as P

LANE = 128


def split_bf16(value):
    hi = lax.reduce_precision(value, exponent_bits=8, mantissa_bits=7)
    rest = value - hi
    mid = lax.reduce_precision(rest, exponent_bits=8, mantissa_bits=7)
    lo = rest - mid
    return [hi, mid, lo]


def per_device(tokens, expert_ids, gate_vals, w_gate, w_up, w_down):
    hid = lax.axis_size("hidden")
    exp = lax.axis_size("expert")
    tok_rows, feat = tokens.shape
    top = expert_ids.shape[1]
    groups = hid * exp
    half = tok_rows // 2
    me = lax.axis_index("expert")
    core = me % 2
    pairs = [(i, i ^ 1) for i in range(exp)]

    route = [expert_ids.astype(jnp.float32)] + split_bf16(gate_vals)
    route = jnp.concatenate(route, axis=1)
    route = jnp.pad(route, ((0, 0), (0, LANE - route.shape[1])))
    wide = jnp.concatenate([tokens, route.astype(jnp.bfloat16)], axis=1)
    width = wide.shape[1]

    halves = wide.reshape(1, 1, 2, half, width)
    spread = jnp.broadcast_to(halves, (hid, exp // 2, 2, half, width)).reshape(groups, half, width)
    mine = lax.all_to_all(spread, ("hidden", "expert"), 0, 0, tiled=True)
    theirs = lax.ppermute(mine, "expert", perm=pairs)
    first = jnp.where(core == 0, mine, theirs)
    second = jnp.where(core == 0, theirs, mine)
    full = jnp.concatenate([first, second], axis=1).reshape(hid, exp, tok_rows, width)

    every_token = full[..., :feat].transpose(0, 2, 1, 3).reshape(hid * tok_rows, exp * feat)
    routing = full[:, 0, :, feat : feat + 4 * top].astype(jnp.float32).reshape(hid * tok_rows, 4 * top)
    ids = routing[:, :top]
    gates = routing[:, top : 2 * top] + routing[:, 2 * top : 3 * top] + routing[:, 3 * top : 4 * top]
    weight = jnp.sum(jnp.where(ids == me.astype(jnp.float32), gates, 0.0), axis=1)

    gate_part = jnp.dot(every_token, w_gate[0], preferred_element_type=jnp.float32)
    up_part = jnp.dot(every_token, w_up[0], preferred_element_type=jnp.float32)
    hidden = (jax.nn.silu(gate_part) * up_part).astype(jnp.bfloat16)
    partial = jnp.dot(hidden, w_down[0], preferred_element_type=jnp.float32)
    weighted = (partial * weight[:, None]).reshape(hid, 2, half, exp * feat)

    keep = jnp.where(core == 0, weighted[:, 0], weighted[:, 1])
    give = jnp.where(core == 0, weighted[:, 1], weighted[:, 0])
    chip_sum = keep + lax.ppermute(give, "expert", perm=pairs)

    outgoing = (
        chip_sum.astype(jnp.bfloat16)
        .reshape(hid, half, exp, feat)
        .transpose(0, 2, 1, 3)
        .reshape(groups, half, feat)
    )
    incoming = lax.all_to_all(outgoing, ("hidden", "expert"), 0, 0, tiled=True)
    incoming = incoming.reshape(hid, exp // 2, 2, half, feat).astype(jnp.float32)
    mixed = jnp.sum(incoming, axis=(0, 1)).reshape(tok_rows, feat)
    return mixed.astype(jnp.bfloat16)


def solution(mesh):
    placed = (
        P("hidden", "expert"),
        P("hidden", None),
        P("hidden", None),
        P("expert", None, "hidden"),
        P("expert", None, "hidden"),
        P("expert", "hidden", None),
    )
    return jax.shard_map(
        per_device, mesh=mesh, in_specs=placed, out_specs=P("hidden", "expert"), check_vma=False
    )
```

```python
import jax
import jax.numpy as jnp
from jax import lax
from jax.sharding import PartitionSpec as P

LANE = 128


def split_bf16(value):
    hi = lax.reduce_precision(value, exponent_bits=8, mantissa_bits=7)
    rest = value - hi
    mid = lax.reduce_precision(rest, exponent_bits=8, mantissa_bits=7)
    lo = rest - mid
    return [hi, mid, lo]


def per_device(tokens, expert_ids, gate_vals, w_gate, w_up, w_down):
    hid = lax.axis_size("hidden")
    exp = lax.axis_size("expert")
    tok_rows, feat = tokens.shape
    top = expert_ids.shape[1]
    groups = hid * exp
    half = tok_rows // 2
    me = lax.axis_index("expert")
    core = me % 2
    pairs = [(i, i ^ 1) for i in range(exp)]

    route = [expert_ids.astype(jnp.float32)] + split_bf16(gate_vals)
    route = jnp.concatenate(route, axis=1)
    route = jnp.pad(route, ((0, 0), (0, LANE - route.shape[1])))
    wide = jnp.concatenate([tokens, route.astype(jnp.bfloat16)], axis=1)
    width = wide.shape[1]

    halves = wide.reshape(1, 1, 2, half, width)
    spread = jnp.broadcast_to(halves, (hid, exp // 2, 2, half, width)).reshape(groups, half, width)
    mine = lax.all_to_all(spread, ("hidden", "expert"), 0, 0, tiled=True)
    theirs = lax.ppermute(mine, "expert", perm=pairs)
    first = jnp.where(core == 0, mine, theirs)
    second = jnp.where(core == 0, theirs, mine)
    full = jnp.concatenate([first, second], axis=1).reshape(hid, exp, tok_rows, width)

    every_token = full[..., :feat].transpose(0, 2, 1, 3).reshape(hid * tok_rows, exp * feat)
    routing = full[:, 0, :, feat : feat + 4 * top].astype(jnp.float32).reshape(hid * tok_rows, 4 * top)
    ids = routing[:, :top]
    gates = routing[:, top : 2 * top] + routing[:, 2 * top : 3 * top] + routing[:, 3 * top : 4 * top]
    weight = jnp.sum(jnp.where(ids == me.astype(jnp.float32), gates, 0.0), axis=1)

    gate_part = jnp.dot(every_token, w_gate[0], preferred_element_type=jnp.float32)
    up_part = jnp.dot(every_token, w_up[0], preferred_element_type=jnp.float32)
    hidden = lax.optimization_barrier((jax.nn.silu(gate_part) * up_part).astype(jnp.bfloat16))
    partial = jnp.dot(hidden, w_down[0], preferred_element_type=jnp.float32)
    weighted = (partial * weight[:, None]).reshape(hid, 2, half, exp * feat)

    keep = jnp.where(core == 0, weighted[:, 0], weighted[:, 1])
    give = jnp.where(core == 0, weighted[:, 1], weighted[:, 0])
    chip_sum = keep + lax.ppermute(give, "expert", perm=pairs)

    outgoing = (
        chip_sum.astype(jnp.bfloat16)
        .reshape(hid, half, exp, feat)
        .transpose(0, 2, 1, 3)
        .reshape(groups, half, feat)
    )
    incoming = lax.all_to_all(outgoing, ("hidden", "expert"), 0, 0, tiled=True)
    incoming = incoming.reshape(hid, exp // 2, 2, half, feat).astype(jnp.float32)
    mixed = jnp.sum(incoming, axis=(0, 1)).reshape(tok_rows, feat)
    return mixed.astype(jnp.bfloat16)


def solution(mesh):
    placed = (
        P("hidden", "expert"),
        P("hidden", None),
        P("hidden", None),
        P("expert", None, "hidden"),
        P("expert", None, "hidden"),
        P("expert", "hidden", None),
    )
    return jax.shard_map(
        per_device, mesh=mesh, in_specs=placed, out_specs=P("hidden", "expert"), check_vma=False
    )
```

```python
import jax
import jax.numpy as jnp
from jax import lax
from jax.sharding import PartitionSpec as P

LANE = 128


def per_device(tokens, expert_ids, gate_vals, w_gate, w_up, w_down):
    hid = lax.axis_size("hidden")
    exp = lax.axis_size("expert")
    tok_rows, feat = tokens.shape
    top = expert_ids.shape[1]
    groups = hid * exp
    half = tok_rows // 2
    me = lax.axis_index("expert")
    core = me % 2
    pairs = [(i, i ^ 1) for i in range(exp)]

    ids_f = expert_ids.astype(jnp.float32)
    cols = jnp.concatenate([ids_f, gate_vals, gate_vals, gate_vals], axis=1)
    hi = lax.reduce_precision(cols, exponent_bits=8, mantissa_bits=7)
    mid = lax.reduce_precision(cols - hi, exponent_bits=8, mantissa_bits=7)
    lo = cols - hi - mid
    group = lax.broadcasted_iota(jnp.int32, cols.shape, 1) // top
    route = jnp.where(group == 0, cols, jnp.where(group == 1, hi, jnp.where(group == 2, mid, lo)))
    route = jnp.pad(route, ((0, 0), (0, LANE - route.shape[1])))
    wide = jnp.concatenate([tokens, route.astype(jnp.bfloat16)], axis=1)
    width = wide.shape[1]

    halves = wide.reshape(1, 1, 2, half, width)
    spread = jnp.broadcast_to(halves, (hid, exp // 2, 2, half, width)).reshape(groups, half, width)
    mine = lax.all_to_all(spread, ("hidden", "expert"), 0, 0, tiled=True)
    theirs = lax.ppermute(mine, "expert", perm=pairs)
    first = jnp.where(core == 0, mine, theirs)
    second = jnp.where(core == 0, theirs, mine)
    full = jnp.concatenate([first, second], axis=1).reshape(hid, exp, tok_rows, width)

    token_pieces = full[..., :feat]
    routing = full[:, 0, :, feat : feat + 4 * top].astype(jnp.float32).reshape(hid * tok_rows, 4 * top)
    ids = routing[:, :top]
    gates = routing[:, top : 2 * top] + routing[:, 2 * top : 3 * top] + routing[:, 3 * top : 4 * top]
    weight = jnp.sum(jnp.where(ids == me.astype(jnp.float32), gates, 0.0), axis=1)

    ff = w_gate.shape[2]

    def project(weights):
        blocks = weights[0].reshape(exp, feat, ff)
        out = jnp.einsum("herf,efn->hrn", token_pieces, blocks, preferred_element_type=jnp.float32)
        return out.reshape(hid * tok_rows, ff)

    gate_part = project(w_gate)
    up_part = project(w_up)
    hidden = lax.optimization_barrier((jax.nn.silu(gate_part) * up_part).astype(jnp.bfloat16))
    partial = jnp.dot(hidden, w_down[0], preferred_element_type=jnp.float32)
    weighted = (partial * weight[:, None]).reshape(hid, 2, half, exp * feat)

    keep = jnp.where(core == 0, weighted[:, 0], weighted[:, 1])
    give = jnp.where(core == 0, weighted[:, 1], weighted[:, 0])
    chip_sum = keep + lax.ppermute(give, "expert", perm=pairs)

    outgoing = (
        chip_sum.astype(jnp.bfloat16)
        .reshape(hid, half, exp, feat)
        .transpose(0, 2, 1, 3)
        .reshape(groups, half, feat)
    )
    incoming = lax.all_to_all(outgoing, ("hidden", "expert"), 0, 0, tiled=True)
    incoming = incoming.reshape(hid, exp // 2, 2, half, feat).astype(jnp.float32)
    mixed = jnp.sum(incoming, axis=(0, 1)).reshape(tok_rows, feat)
    return mixed.astype(jnp.bfloat16)


def solution(mesh):
    placed = (
        P("hidden", "expert"),
        P("hidden", None),
        P("hidden", None),
        P("expert", None, "hidden"),
        P("expert", None, "hidden"),
        P("expert", "hidden", None),
    )
    return jax.shard_map(
        per_device, mesh=mesh, in_specs=placed, out_specs=P("hidden", "expert"), check_vma=False
    )
```

```python
import jax
import jax.numpy as jnp
from jax import lax
from jax.experimental import pallas as pl
from jax.sharding import PartitionSpec as P

LANE = 128
FF_STEP = 256
ROW_STEP = 256


def expert_kernel(x_ref, wg_ref, wu_ref, wd_ref, w_ref, out_ref):
    step = pl.program_id(1)
    pieces, _, _ = x_ref.shape
    feat = wg_ref.shape[0] // pieces
    gate = None
    up = None
    for p in range(pieces):
        x = x_ref[p, :, :feat]
        g = jnp.dot(x, wg_ref[p * feat : (p + 1) * feat, :], preferred_element_type=jnp.float32)
        u = jnp.dot(x, wu_ref[p * feat : (p + 1) * feat, :], preferred_element_type=jnp.float32)
        gate = g if gate is None else gate + g
        up = u if up is None else up + u
    hidden = (gate / (1.0 + jnp.exp(-gate)) * up).astype(jnp.bfloat16)
    down = jnp.dot(hidden, wd_ref[...], preferred_element_type=jnp.float32)

    @pl.when(step == 0)
    def _():
        out_ref[...] = down

    @pl.when(step > 0)
    def _():
        out_ref[...] += down

    @pl.when(step == pl.num_programs(1) - 1)
    def _():
        out_ref[...] = out_ref[...] * w_ref[...]


def expert_ffn(x, w_gate, w_up, w_down, weight):
    pieces, rows, width = x.shape
    dim, ff = w_gate.shape
    ff_step = min(FF_STEP, ff)
    row_step = min(ROW_STEP, rows)
    grid = (rows // row_step, ff // ff_step)
    return pl.pallas_call(
        expert_kernel,
        grid=grid,
        in_specs=[
            pl.BlockSpec((pieces, row_step, width), lambda r, j: (0, r, 0)),
            pl.BlockSpec((dim, ff_step), lambda r, j: (0, j)),
            pl.BlockSpec((dim, ff_step), lambda r, j: (0, j)),
            pl.BlockSpec((ff_step, dim), lambda r, j: (j, 0)),
            pl.BlockSpec((row_step, 1), lambda r, j: (r, 0)),
        ],
        out_specs=pl.BlockSpec((row_step, dim), lambda r, j: (r, 0)),
        out_shape=jax.ShapeDtypeStruct((rows, dim), jnp.float32),
    )(x, w_gate, w_up, w_down, weight)


def per_device(tokens, expert_ids, gate_vals, w_gate, w_up, w_down):
    hid = lax.axis_size("hidden")
    exp = lax.axis_size("expert")
    tok_rows, feat = tokens.shape
    top = expert_ids.shape[1]
    groups = hid * exp
    half = tok_rows // 2
    me = lax.axis_index("expert")
    core = me % 2
    pairs = [(i, i ^ 1) for i in range(exp)]

    ids_f = expert_ids.astype(jnp.float32)
    cols = jnp.concatenate([ids_f, gate_vals, gate_vals, gate_vals], axis=1)
    hi = lax.reduce_precision(cols, exponent_bits=8, mantissa_bits=7)
    mid = lax.reduce_precision(cols - hi, exponent_bits=8, mantissa_bits=7)
    lo = cols - hi - mid
    group = lax.broadcasted_iota(jnp.int32, cols.shape, 1) // top
    route = jnp.where(group == 0, cols, jnp.where(group == 1, hi, jnp.where(group == 2, mid, lo)))
    route = jnp.pad(route, ((0, 0), (0, LANE - route.shape[1])))
    wide = jnp.concatenate([tokens, route.astype(jnp.bfloat16)], axis=1)
    width = wide.shape[1]

    halves = wide.reshape(1, 1, 2, half, width)
    spread = jnp.broadcast_to(halves, (hid, exp // 2, 2, half, width)).reshape(groups, half, width)
    mine = lax.all_to_all(spread, ("hidden", "expert"), 0, 0, tiled=True)
    theirs = lax.ppermute(mine, "expert", perm=pairs)
    both = jnp.stack([mine, theirs]).reshape(2, hid, exp, half, width)
    slabs = both.transpose(2, 0, 1, 3, 4).reshape(exp, 2 * hid * half, width)
    routing = slabs[0, :, feat : feat + 4 * top].astype(jnp.float32)
    ids = routing[:, :top]
    gates = routing[:, top : 2 * top] + routing[:, 2 * top : 3 * top] + routing[:, 3 * top : 4 * top]
    weight = jnp.sum(jnp.where(ids == me.astype(jnp.float32), gates, 0.0), axis=1)

    weighted = expert_ffn(slabs, w_gate[0], w_up[0], w_down[0], weight[:, None])
    weighted = weighted.reshape(2, hid, half, exp * feat)

    chip_sum = weighted[0] + lax.ppermute(weighted[1], "expert", perm=pairs)

    outgoing = (
        chip_sum.astype(jnp.bfloat16)
        .reshape(hid, half, exp, feat)
        .transpose(0, 2, 1, 3)
        .reshape(groups, half, feat)
    )
    incoming = lax.all_to_all(outgoing, ("hidden", "expert"), 0, 0, tiled=True)
    incoming = incoming.reshape(hid, exp // 2, 2, half, feat).astype(jnp.float32)
    mixed = jnp.sum(incoming, axis=(0, 1)).reshape(tok_rows, feat)
    return mixed.astype(jnp.bfloat16)


def solution(mesh):
    placed = (
        P("hidden", "expert"),
        P("hidden", None),
        P("hidden", None),
        P("expert", None, "hidden"),
        P("expert", None, "hidden"),
        P("expert", "hidden", None),
    )
    return jax.shard_map(
        per_device, mesh=mesh, in_specs=placed, out_specs=P("hidden", "expert"), check_vma=False
    )
```

```python
import jax
import jax.numpy as jnp
from jax import lax
from jax.experimental import pallas as pl
from jax.experimental.pallas import tpu as pltpu
from jax.sharding import PartitionSpec as P

LANE = 128
FF_STEP = 256
ROW_STEP = 256


def expert_kernel(x_ref, wg_ref, wu_ref, wd_ref, mask_ref, keep_ref, give_ref, gate_acc, up_acc, hid_scr, acc):
    s = pl.program_id(1)
    pieces, _, rows, width = x_ref.shape
    feat = wg_ref.shape[0]
    ff_step = wd_ref.shape[0]

    @pl.when(s < pieces)
    def _():
        x = x_ref[s].reshape(2 * rows, width)[:, :feat]
        g = jnp.dot(x, wg_ref[...], preferred_element_type=jnp.float32)
        u = jnp.dot(x, wu_ref[...], preferred_element_type=jnp.float32)

        @pl.when(s == 0)
        def _():
            gate_acc[...] = g
            up_acc[...] = u

        @pl.when(s > 0)
        def _():
            gate_acc[...] += g
            up_acc[...] += u

        @pl.when(s == pieces - 1)
        def _():
            gate = gate_acc[...]
            hid_scr[...] = (gate / (1.0 + jnp.exp(-gate)) * up_acc[...]).astype(jnp.bfloat16)

    @pl.when(s >= pieces)
    def _():
        j = s - pieces
        h = hid_scr[:, pl.ds(pl.multiple_of(j * ff_step, ff_step), ff_step)]
        down = jnp.dot(h, wd_ref[...], preferred_element_type=jnp.float32)

        @pl.when(j == 0)
        def _():
            acc[...] = down

        @pl.when(j > 0)
        def _():
            acc[...] += down

    @pl.when(s == pl.num_programs(1) - 1)
    def _():
        route = x_ref[0].reshape(2 * rows, width)[:, feat:].astype(jnp.float32)
        weight = jnp.sum(route * mask_ref[...], axis=1, keepdims=True)
        out = acc[...] * weight
        keep_ref[...] = out[:rows]
        give_ref[...] = out[rows:]


def expert_ffn(x, w_gate, w_up, w_down, mask):
    pieces, _, rows, width = x.shape
    dim, ff = w_gate.shape
    feat = dim // pieces
    ff_step = min(FF_STEP, ff)
    row_step = min(ROW_STEP // 2, rows)
    last = pieces - 1
    grid = (rows // row_step, pieces + ff // ff_step)
    out = jax.ShapeDtypeStruct((rows, dim), jnp.float32)
    return pl.pallas_call(
        expert_kernel,
        grid=grid,
        in_specs=[
            pl.BlockSpec((pieces, 2, row_step, width), lambda r, s: (0, 0, r, 0)),
            pl.BlockSpec((feat, ff), lambda r, s: (jnp.minimum(s, last), 0)),
            pl.BlockSpec((feat, ff), lambda r, s: (jnp.minimum(s, last), 0)),
            pl.BlockSpec((ff_step, dim), lambda r, s: (jnp.maximum(s - pieces, 0), 0)),
            pl.BlockSpec(mask.shape, lambda r, s: (0, 0)),
        ],
        out_specs=[
            pl.BlockSpec((row_step, dim), lambda r, s: (r, 0)),
            pl.BlockSpec((row_step, dim), lambda r, s: (r, 0)),
        ],
        out_shape=[out, out],
        scratch_shapes=[
            pltpu.VMEM((2 * row_step, ff), jnp.float32),
            pltpu.VMEM((2 * row_step, ff), jnp.float32),
            pltpu.VMEM((2 * row_step, ff), jnp.bfloat16),
            pltpu.VMEM((2 * row_step, dim), jnp.float32),
        ],
    )(x, w_gate, w_up, w_down, mask)


def per_device(tokens, expert_ids, gate_vals, w_gate, w_up, w_down):
    hid = lax.axis_size("hidden")
    exp = lax.axis_size("expert")
    tok_rows, feat = tokens.shape
    groups = hid * exp
    half = tok_rows // 2
    me = lax.axis_index("expert")
    pairs = [(i, i ^ 1) for i in range(exp)]

    chosen = expert_ids[:, :, None] == jnp.arange(exp, dtype=expert_ids.dtype)[None, None, :]
    per_expert = jnp.sum(jnp.where(chosen, gate_vals[:, :, None], 0.0), axis=1)
    hi = lax.reduce_precision(per_expert, exponent_bits=8, mantissa_bits=7)
    mid = lax.reduce_precision(per_expert - hi, exponent_bits=8, mantissa_bits=7)
    lo = per_expert - hi - mid
    route = jnp.stack([hi, mid, lo], axis=2).reshape(tok_rows, 3 * exp)
    route = jnp.pad(route, ((0, 0), (0, LANE - route.shape[1])))
    wide = jnp.concatenate([tokens, route.astype(jnp.bfloat16)], axis=1)
    width = wide.shape[1]

    halves = wide.reshape(1, 1, 2, half, width)
    spread = jnp.broadcast_to(halves, (hid, exp // 2, 2, half, width)).reshape(groups, half, width)
    mine = lax.all_to_all(spread, ("hidden", "expert"), 0, 0, tiled=True)
    theirs = lax.ppermute(mine, "expert", perm=pairs)
    both = jnp.stack([mine, theirs]).reshape(2, hid, exp, half, width)
    slabs = both.transpose(2, 0, 1, 3, 4).reshape(exp, 2, hid * half, width)
    lane = jnp.arange(LANE, dtype=jnp.int32)[None, :]
    mask = ((lane // 3 == me) & (lane < 3 * exp)).astype(jnp.float32)

    keep, give = expert_ffn(slabs, w_gate[0], w_up[0], w_down[0], mask)
    keep = keep.reshape(hid, half, exp * feat)
    give = give.reshape(hid, half, exp * feat)

    chip_sum = keep + lax.ppermute(give, "expert", perm=pairs)

    outgoing = (
        chip_sum.astype(jnp.bfloat16)
        .reshape(hid, half, exp, feat)
        .transpose(0, 2, 1, 3)
        .reshape(groups, half, feat)
    )
    incoming = lax.all_to_all(outgoing, ("hidden", "expert"), 0, 0, tiled=True)
    incoming = incoming.reshape(hid, exp // 2, 2, half, feat).astype(jnp.float32)
    mixed = jnp.sum(incoming, axis=(0, 1)).reshape(tok_rows, feat)
    return mixed.astype(jnp.bfloat16)


def solution(mesh):
    placed = (
        P("hidden", "expert"),
        P("hidden", None),
        P("hidden", None),
        P("expert", None, "hidden"),
        P("expert", None, "hidden"),
        P("expert", "hidden", None),
    )
    return jax.shard_map(
        per_device, mesh=mesh, in_specs=placed, out_specs=P("hidden", "expert"), check_vma=False
    )
```

```python
import jax
import jax.numpy as jnp
from jax import lax
from jax.sharding import PartitionSpec as P

LANE = 128


def per_device(tokens, expert_ids, gate_vals, w_gate, w_up, w_down):
    hid = lax.axis_size("hidden")
    exp = lax.axis_size("expert")
    tok_rows, feat = tokens.shape
    top = expert_ids.shape[1]
    groups = hid * exp
    half = tok_rows // 2
    me = lax.axis_index("expert")
    core = me % 2
    pairs = [(i, i ^ 1) for i in range(exp)]

    experts = jnp.arange(exp, dtype=expert_ids.dtype)[None, :]
    per_expert = jnp.where(expert_ids[:, :1] == experts, gate_vals[:, :1], 0.0)
    for k in range(1, top):
        per_expert = per_expert + jnp.where(expert_ids[:, k : k + 1] == experts, gate_vals[:, k : k + 1], 0.0)
    hi = lax.reduce_precision(per_expert, exponent_bits=8, mantissa_bits=7)
    mid = lax.reduce_precision(per_expert - hi, exponent_bits=8, mantissa_bits=7)
    lo = per_expert - hi - mid
    route = jnp.stack([hi, mid, lo], axis=2).reshape(tok_rows, 3 * exp)
    route = jnp.pad(route, ((0, 0), (0, LANE - route.shape[1])))
    wide = jnp.concatenate([tokens, route.astype(jnp.bfloat16)], axis=1)
    width = wide.shape[1]

    halves = wide.reshape(1, 1, 2, half, width)
    spread = jnp.broadcast_to(halves, (hid, exp // 2, 2, half, width)).reshape(groups, half, width)
    mine = lax.all_to_all(spread, ("hidden", "expert"), 0, 0, tiled=True)
    theirs = lax.ppermute(mine, "expert", perm=pairs)
    first = jnp.where(core == 0, mine, theirs)
    second = jnp.where(core == 0, theirs, mine)
    full = jnp.concatenate([first, second], axis=1).reshape(hid, exp, tok_rows, width)

    token_pieces = full[..., :feat]
    routing = full[:, 0, :, feat:].astype(jnp.float32).reshape(hid * tok_rows, LANE)
    lane = jnp.arange(LANE, dtype=jnp.int32)[None, :]
    weight = jnp.sum(jnp.where(lane // 3 == me, routing, 0.0), axis=1)

    ff = w_gate.shape[2]

    def project(weights):
        blocks = weights[0].reshape(exp, feat, ff)
        out = jnp.einsum("herf,efn->hrn", token_pieces, blocks, preferred_element_type=jnp.float32)
        return out.reshape(hid * tok_rows, ff)

    gate_part = project(w_gate)
    up_part = project(w_up)
    hidden = lax.optimization_barrier((jax.nn.silu(gate_part) * up_part).astype(jnp.bfloat16))
    partial = jnp.dot(hidden, w_down[0], preferred_element_type=jnp.float32)
    weighted = (partial * weight[:, None]).reshape(hid, 2, half, exp * feat)

    keep = jnp.where(core == 0, weighted[:, 0], weighted[:, 1])
    give = jnp.where(core == 0, weighted[:, 1], weighted[:, 0])
    chip_sum = keep + lax.ppermute(give, "expert", perm=pairs)

    outgoing = (
        chip_sum.astype(jnp.bfloat16)
        .reshape(hid, half, exp, feat)
        .transpose(0, 2, 1, 3)
        .reshape(groups, half, feat)
    )
    incoming = lax.all_to_all(outgoing, ("hidden", "expert"), 0, 0, tiled=True)
    incoming = incoming.reshape(hid, exp // 2, 2, half, feat).astype(jnp.float32)
    mixed = jnp.sum(incoming, axis=(0, 1)).reshape(tok_rows, feat)
    return mixed.astype(jnp.bfloat16)


def solution(mesh):
    placed = (
        P("hidden", "expert"),
        P("hidden", None),
        P("hidden", None),
        P("expert", None, "hidden"),
        P("expert", None, "hidden"),
        P("expert", "hidden", None),
    )
    return jax.shard_map(
        per_device, mesh=mesh, in_specs=placed, out_specs=P("hidden", "expert"), check_vma=False
    )
```

```python
import jax
import jax.numpy as jnp
from jax import lax
from jax.sharding import PartitionSpec as P

LANE = 128


def per_device(tokens, expert_ids, gate_vals, w_gate, w_up, w_down):
    hid = lax.axis_size("hidden")
    exp = lax.axis_size("expert")
    tok_rows, feat = tokens.shape
    top = expert_ids.shape[1]
    groups = hid * exp
    half = tok_rows // 2
    me = lax.axis_index("expert")
    pairs = [(i, i ^ 1) for i in range(exp)]

    ids_f = expert_ids.astype(jnp.float32)
    cols = jnp.concatenate([ids_f, gate_vals, gate_vals, gate_vals], axis=1)
    hi = lax.reduce_precision(cols, exponent_bits=8, mantissa_bits=7)
    mid = lax.reduce_precision(cols - hi, exponent_bits=8, mantissa_bits=7)
    lo = cols - hi - mid
    group = lax.broadcasted_iota(jnp.int32, cols.shape, 1) // top
    route = jnp.where(group == 0, cols, jnp.where(group == 1, hi, jnp.where(group == 2, mid, lo)))
    route = jnp.pad(route, ((0, 0), (0, LANE - route.shape[1])))
    wide = jnp.concatenate([tokens, route.astype(jnp.bfloat16)], axis=1)
    width = wide.shape[1]

    halves = wide.reshape(1, 1, 2, half, width)
    spread = jnp.broadcast_to(halves, (hid, exp // 2, 2, half, width)).reshape(groups, half, width)
    mine = lax.all_to_all(spread, ("hidden", "expert"), 0, 0, tiled=True)
    theirs = lax.ppermute(mine, "expert", perm=pairs)
    ff = w_gate.shape[2]
    gate_w = w_gate[0].reshape(exp, feat, ff)
    up_w = w_up[0].reshape(exp, feat, ff)
    top_lanes = 4 * top

    def expert_rows(got):
        got = got.reshape(hid, exp, half, width)
        pieces = got[..., :feat]
        routing = got[:, 0, :, feat : feat + top_lanes].astype(jnp.float32).reshape(hid * half, top_lanes)
        ids = routing[:, :top]
        gates = routing[:, top : 2 * top] + routing[:, 2 * top : 3 * top] + routing[:, 3 * top : 4 * top]
        weight = jnp.sum(jnp.where(ids == me.astype(jnp.float32), gates, 0.0), axis=1)
        gate_part = jnp.einsum("herf,efn->hrn", pieces, gate_w, preferred_element_type=jnp.float32)
        up_part = jnp.einsum("herf,efn->hrn", pieces, up_w, preferred_element_type=jnp.float32)
        hidden = (jax.nn.silu(gate_part) * up_part).astype(jnp.bfloat16).reshape(hid * half, ff)
        hidden = lax.optimization_barrier(hidden)
        partial = jnp.dot(hidden, w_down[0], preferred_element_type=jnp.float32)
        return (partial * weight[:, None]).reshape(hid, half, exp * feat)

    keep = expert_rows(mine)
    give = expert_rows(theirs)
    chip_sum = keep + lax.ppermute(give, "expert", perm=pairs)

    outgoing = (
        chip_sum.astype(jnp.bfloat16)
        .reshape(hid, half, exp, feat)
        .transpose(0, 2, 1, 3)
        .reshape(groups, half, feat)
    )
    incoming = lax.all_to_all(outgoing, ("hidden", "expert"), 0, 0, tiled=True)
    incoming = incoming.reshape(hid, exp // 2, 2, half, feat).astype(jnp.float32)
    mixed = jnp.sum(incoming, axis=(0, 1)).reshape(tok_rows, feat)
    return mixed.astype(jnp.bfloat16)


def solution(mesh):
    placed = (
        P("hidden", "expert"),
        P("hidden", None),
        P("hidden", None),
        P("expert", None, "hidden"),
        P("expert", None, "hidden"),
        P("expert", "hidden", None),
    )
    return jax.shard_map(
        per_device, mesh=mesh, in_specs=placed, out_specs=P("hidden", "expert"), check_vma=False
    )
```

```python
import jax
import jax.numpy as jnp
from jax import lax
from jax.sharding import PartitionSpec as P

def per_device(tokens, expert_ids, gate_vals, w_gate, w_up, w_down):
    hid = lax.axis_size("hidden")
    exp = lax.axis_size("expert")
    tok_rows, feat = tokens.shape
    top = expert_ids.shape[1]
    groups = hid * exp
    half = tok_rows // 2
    me = lax.axis_index("expert")
    core = me % 2
    pairs = [(i, i ^ 1) for i in range(exp)]

    weight = jnp.sum(jnp.where(expert_ids == me, gate_vals, 0.0), axis=1)[None, :]
    hi = lax.axis_index("hidden")
    have = 1
    while have < hid:
        shift = min(have, hid - have)
        moved = lax.ppermute(weight[:shift], "hidden", perm=[(j, (j + have) % hid) for j in range(hid)])
        weight = jnp.concatenate([weight, moved], axis=0)
        have += shift
    weight = jnp.take(weight, (hi - jnp.arange(hid)) % hid, axis=0).reshape(hid * tok_rows)
    wide = tokens
    width = feat

    halves = wide.reshape(1, 1, 2, half, width)
    spread = jnp.broadcast_to(halves, (hid, exp // 2, 2, half, width)).reshape(groups, half, width)
    mine = lax.all_to_all(spread, ("hidden", "expert"), 0, 0, tiled=True)
    theirs = lax.ppermute(mine, "expert", perm=pairs)
    first = jnp.where(core == 0, mine, theirs)
    second = jnp.where(core == 0, theirs, mine)
    full = jnp.concatenate([first, second], axis=1).reshape(hid, exp, tok_rows, width)

    token_pieces = full
    ff = w_gate.shape[2]

    def project(weights):
        blocks = weights[0].reshape(exp, feat, ff)
        out = jnp.einsum("herf,efn->hrn", token_pieces, blocks, preferred_element_type=jnp.float32)
        return out.reshape(hid * tok_rows, ff)

    gate_part = project(w_gate)
    up_part = project(w_up)
    hidden = lax.optimization_barrier((jax.nn.silu(gate_part) * up_part).astype(jnp.bfloat16))
    partial = jnp.dot(hidden, w_down[0], preferred_element_type=jnp.float32)
    weighted = (partial * weight[:, None]).reshape(hid, 2, half, exp * feat)

    keep = jnp.where(core == 0, weighted[:, 0], weighted[:, 1])
    give = jnp.where(core == 0, weighted[:, 1], weighted[:, 0])
    chip_sum = keep + lax.ppermute(give, "expert", perm=pairs)

    outgoing = (
        chip_sum.astype(jnp.bfloat16)
        .reshape(hid, half, exp, feat)
        .transpose(0, 2, 1, 3)
        .reshape(groups, half, feat)
    )
    incoming = lax.all_to_all(outgoing, ("hidden", "expert"), 0, 0, tiled=True)
    incoming = incoming.reshape(hid, exp // 2, 2, half, feat).astype(jnp.float32)
    mixed = jnp.sum(incoming, axis=(0, 1)).reshape(tok_rows, feat)
    return mixed.astype(jnp.bfloat16)


def solution(mesh):
    placed = (
        P("hidden", "expert"),
        P("hidden", None),
        P("hidden", None),
        P("expert", None, "hidden"),
        P("expert", None, "hidden"),
        P("expert", "hidden", None),
    )
    return jax.shard_map(
        per_device, mesh=mesh, in_specs=placed, out_specs=P("hidden", "expert"), check_vma=False
    )
```

```python
import jax
import jax.numpy as jnp
from jax import lax
from jax.sharding import PartitionSpec as P

LANE = 128


def per_device(tokens, expert_ids, gate_vals, w_gate, w_up, w_down):
    hid = lax.axis_size("hidden")
    exp = lax.axis_size("expert")
    tok_rows, feat = tokens.shape
    top = expert_ids.shape[1]
    groups = hid * exp
    half = tok_rows // 2
    me = lax.axis_index("expert")
    core = me % 2
    pairs = [(i, i ^ 1) for i in range(exp)]

    lane = lax.broadcasted_iota(jnp.int32, (tok_rows, LANE), 1)
    which = lane % top
    group = lane // top
    ids_cols = jnp.zeros((tok_rows, LANE), jnp.float32)
    gate_cols = jnp.zeros((tok_rows, LANE), jnp.float32)
    for k in range(top):
        ids_cols = jnp.where(which == k, expert_ids[:, k : k + 1].astype(jnp.float32), ids_cols)
        gate_cols = jnp.where(which == k, gate_vals[:, k : k + 1], gate_cols)
    hi = lax.reduce_precision(gate_cols, exponent_bits=8, mantissa_bits=7)
    mid = lax.reduce_precision(gate_cols - hi, exponent_bits=8, mantissa_bits=7)
    lo = gate_cols - hi - mid
    route = jnp.where(group == 0, ids_cols, jnp.where(group == 1, hi, jnp.where(group == 2, mid, lo)))
    route = jnp.where(group < 4, route, 0.0)
    wide = jnp.concatenate([tokens, route.astype(jnp.bfloat16)], axis=1)
    width = wide.shape[1]

    halves = wide.reshape(1, 1, 2, half, width)
    spread = jnp.broadcast_to(halves, (hid, exp // 2, 2, half, width)).reshape(groups, half, width)
    mine = lax.all_to_all(spread, ("hidden", "expert"), 0, 0, tiled=True)
    theirs = lax.ppermute(mine, "expert", perm=pairs)
    first = jnp.where(core == 0, mine, theirs)
    second = jnp.where(core == 0, theirs, mine)
    full = jnp.concatenate([first, second], axis=1).reshape(hid, exp, tok_rows, width)

    token_pieces = full[..., :feat]
    routing = full[:, 0, :, feat : feat + 4 * top].astype(jnp.float32).reshape(hid * tok_rows, 4 * top)
    ids = routing[:, :top]
    gates = routing[:, top : 2 * top] + routing[:, 2 * top : 3 * top] + routing[:, 3 * top : 4 * top]
    weight = jnp.sum(jnp.where(ids == me.astype(jnp.float32), gates, 0.0), axis=1)

    ff = w_gate.shape[2]

    def project(weights):
        blocks = weights[0].reshape(exp, feat, ff)
        out = jnp.einsum("herf,efn->hrn", token_pieces, blocks, preferred_element_type=jnp.float32)
        return out.reshape(hid * tok_rows, ff)

    gate_part = project(w_gate)
    up_part = project(w_up)
    hidden = lax.optimization_barrier((jax.nn.silu(gate_part) * up_part).astype(jnp.bfloat16))
    partial = jnp.dot(hidden, w_down[0], preferred_element_type=jnp.float32)
    weighted = (partial * weight[:, None]).reshape(hid, 2, half, exp * feat)

    keep = jnp.where(core == 0, weighted[:, 0], weighted[:, 1])
    give = jnp.where(core == 0, weighted[:, 1], weighted[:, 0])
    chip_sum = keep + lax.ppermute(give, "expert", perm=pairs)

    outgoing = (
        chip_sum.astype(jnp.bfloat16)
        .reshape(hid, half, exp, feat)
        .transpose(0, 2, 1, 3)
        .reshape(groups, half, feat)
    )
    incoming = lax.all_to_all(outgoing, ("hidden", "expert"), 0, 0, tiled=True)
    incoming = incoming.reshape(hid, exp // 2, 2, half, feat).astype(jnp.float32)
    mixed = jnp.sum(incoming, axis=(0, 1)).reshape(tok_rows, feat)
    return mixed.astype(jnp.bfloat16)


def solution(mesh):
    placed = (
        P("hidden", "expert"),
        P("hidden", None),
        P("hidden", None),
        P("expert", None, "hidden"),
        P("expert", None, "hidden"),
        P("expert", "hidden", None),
    )
    return jax.shard_map(
        per_device, mesh=mesh, in_specs=placed, out_specs=P("hidden", "expert"), check_vma=False
    )
```

```python
import jax
import jax.numpy as jnp
from jax import lax
from jax.sharding import PartitionSpec as P

LANE = 128


def per_device(tokens, expert_ids, gate_vals, w_gate, w_up, w_down):
    hid = lax.axis_size("hidden")
    exp = lax.axis_size("expert")
    tok_rows, feat = tokens.shape
    top = expert_ids.shape[1]
    groups = hid * exp
    half = tok_rows // 2
    me = lax.axis_index("expert")
    core = me % 2
    pairs = [(i, i ^ 1) for i in range(exp)]

    ids_f = expert_ids.astype(jnp.float32)
    cols = jnp.concatenate([ids_f, gate_vals, gate_vals, gate_vals], axis=1)
    hi = lax.reduce_precision(cols, exponent_bits=8, mantissa_bits=7)
    mid = lax.reduce_precision(cols - hi, exponent_bits=8, mantissa_bits=7)
    lo = cols - hi - mid
    group = lax.broadcasted_iota(jnp.int32, cols.shape, 1) // top
    route = jnp.where(group == 0, cols, jnp.where(group == 1, hi, jnp.where(group == 2, mid, lo)))
    route = jnp.pad(route, ((0, 0), (0, LANE - route.shape[1])))
    wide = jnp.concatenate([tokens, route.astype(jnp.bfloat16)], axis=1)
    width = wide.shape[1]

    halves = wide.reshape(1, 1, 2, half, width)
    spread = jnp.broadcast_to(halves, (hid, exp // 2, 2, half, width)).reshape(groups, half, width)
    mine = lax.all_to_all(spread, ("hidden", "expert"), 0, 0, tiled=True)
    theirs = lax.ppermute(mine, "expert", perm=pairs)
    first = jnp.where(core == 0, mine, theirs)
    second = jnp.where(core == 0, theirs, mine)
    full = jnp.concatenate([first, second], axis=1).reshape(hid, exp, tok_rows, width)

    token_pieces = full[..., :feat]
    routing = full[:, 0, :, feat : feat + 4 * top].astype(jnp.float32).reshape(hid * tok_rows, 4 * top)
    ids = routing[:, :top]
    gates = routing[:, top : 2 * top] + routing[:, 2 * top : 3 * top] + routing[:, 3 * top : 4 * top]
    weight = jnp.sum(jnp.where(ids == me.astype(jnp.float32), gates, 0.0), axis=1)

    ff = w_gate.shape[2]

    def project(weights):
        blocks = weights[0].reshape(exp, feat, ff)
        out = jnp.einsum("herf,efn->hrn", token_pieces, blocks, preferred_element_type=jnp.float32)
        return out.reshape(hid * tok_rows, ff)

    gate_part = project(w_gate)
    up_part = project(w_up)
    hidden = lax.optimization_barrier((jax.nn.silu(gate_part) * up_part).astype(jnp.bfloat16))
    rows_by_half = hidden.reshape(hid, 2, half, ff)
    weight_by_half = weight.reshape(hid, 2, half, 1)
    give_rows = jnp.where(core == 0, rows_by_half[:, 1], rows_by_half[:, 0]).reshape(hid * half, ff)
    keep_rows = jnp.where(core == 0, rows_by_half[:, 0], rows_by_half[:, 1]).reshape(hid * half, ff)
    give_w = jnp.where(core == 0, weight_by_half[:, 1], weight_by_half[:, 0])
    keep_w = jnp.where(core == 0, weight_by_half[:, 0], weight_by_half[:, 1])
    give = jnp.dot(give_rows, w_down[0], preferred_element_type=jnp.float32).reshape(hid, half, -1) * give_w
    keep = lax.optimization_barrier(jnp.dot(keep_rows, w_down[0], preferred_element_type=jnp.float32).reshape(hid, half, -1) * keep_w)
    chip_sum = keep + lax.ppermute(give, "expert", perm=pairs)

    outgoing = (
        chip_sum.astype(jnp.bfloat16)
        .reshape(hid, half, exp, feat)
        .transpose(0, 2, 1, 3)
        .reshape(groups, half, feat)
    )
    incoming = lax.all_to_all(outgoing, ("hidden", "expert"), 0, 0, tiled=True)
    incoming = incoming.reshape(hid, exp // 2, 2, half, feat).astype(jnp.float32)
    mixed = jnp.sum(incoming, axis=(0, 1)).reshape(tok_rows, feat)
    return mixed.astype(jnp.bfloat16)


def solution(mesh):
    placed = (
        P("hidden", "expert"),
        P("hidden", None),
        P("hidden", None),
        P("expert", None, "hidden"),
        P("expert", None, "hidden"),
        P("expert", "hidden", None),
    )
    return jax.shard_map(
        per_device, mesh=mesh, in_specs=placed, out_specs=P("hidden", "expert"), check_vma=False
    )
```

```python
import jax
import jax.numpy as jnp
from jax import lax
from jax.experimental import pallas as pl
from jax.experimental.pallas import tpu as pltpu
from jax.sharding import PartitionSpec as P

LANE = 128
DOWN_CHUNKS = 4


def ffn_kernel(x_ref, wg_hbm, wu_hbm, wd_hbm, out_ref, wg_v, wu_v, wd_v, sems):
    pieces, _, _ = x_ref.shape
    feat = wg_v.shape[1]
    ff = wd_v.shape[0]
    step = ff // DOWN_CHUNKS
    gate_copies = []
    down_copies = []
    for p in range(pieces):
        rows = pl.ds(p * feat, feat)
        gate_copies.append((
            pltpu.make_async_copy(wg_hbm.at[rows], wg_v.at[p], sems.at[2 * p]),
            pltpu.make_async_copy(wu_hbm.at[rows], wu_v.at[p], sems.at[2 * p + 1]),
        ))
    for c in range(DOWN_CHUNKS):
        rows = pl.ds(c * step, step)
        down_copies.append(pltpu.make_async_copy(wd_hbm.at[rows], wd_v.at[rows], sems.at[2 * pieces + c]))
    for g, u in gate_copies:
        g.start()
        u.start()
    for d in down_copies:
        d.start()
    gate = None
    up = None
    for p in range(pieces):
        g, u = gate_copies[p]
        g.wait()
        u.wait()
        x = x_ref[p][:, :feat]
        gp = jnp.dot(x, wg_v[p], preferred_element_type=jnp.float32)
        up_p = jnp.dot(x, wu_v[p], preferred_element_type=jnp.float32)
        gate = gp if gate is None else gate + gp
        up = up_p if up is None else up + up_p
    hidden = (gate / (1.0 + jnp.exp(-gate)) * up).astype(jnp.bfloat16)
    acc = None
    for c in range(DOWN_CHUNKS):
        down_copies[c].wait()
        d = jnp.dot(hidden[:, c * step : (c + 1) * step], wd_v[c * step : (c + 1) * step, :], preferred_element_type=jnp.float32)
        acc = d if acc is None else acc + d
    out_ref[...] = acc


def expert_ffn(x, w_gate, w_up, w_down):
    pieces, rows, _ = x.shape
    dim, ff = w_gate.shape
    feat = dim // pieces
    vmem = pl.BlockSpec(memory_space=pltpu.VMEM)
    hbm = pl.BlockSpec(memory_space=pl.ANY)
    return pl.pallas_call(
        ffn_kernel,
        in_specs=[vmem, hbm, hbm, hbm],
        out_specs=vmem,
        out_shape=jax.ShapeDtypeStruct((rows, dim), jnp.float32),
        scratch_shapes=[
            pltpu.VMEM((pieces, feat, ff), w_gate.dtype),
            pltpu.VMEM((pieces, feat, ff), w_up.dtype),
            pltpu.VMEM((ff, dim), w_down.dtype),
            pltpu.SemaphoreType.DMA((2 * pieces + DOWN_CHUNKS,)),
        ],
    )(x, w_gate, w_up, w_down)


def per_device(tokens, expert_ids, gate_vals, w_gate, w_up, w_down):
    hid = lax.axis_size("hidden")
    exp = lax.axis_size("expert")
    tok_rows, feat = tokens.shape
    top = expert_ids.shape[1]
    groups = hid * exp
    half = tok_rows // 2
    me = lax.axis_index("expert")
    core = me % 2
    pairs = [(i, i ^ 1) for i in range(exp)]

    ids_f = expert_ids.astype(jnp.float32)
    cols = jnp.concatenate([ids_f, gate_vals, gate_vals, gate_vals], axis=1)
    hi = lax.reduce_precision(cols, exponent_bits=8, mantissa_bits=7)
    mid = lax.reduce_precision(cols - hi, exponent_bits=8, mantissa_bits=7)
    lo = cols - hi - mid
    group = lax.broadcasted_iota(jnp.int32, cols.shape, 1) // top
    route = jnp.where(group == 0, cols, jnp.where(group == 1, hi, jnp.where(group == 2, mid, lo)))
    route = jnp.pad(route, ((0, 0), (0, LANE - route.shape[1])))
    wide = jnp.concatenate([tokens, route.astype(jnp.bfloat16)], axis=1)
    width = wide.shape[1]

    halves = wide.reshape(1, 1, 2, half, width)
    spread = jnp.broadcast_to(halves, (hid, exp // 2, 2, half, width)).reshape(groups, half, width)
    mine = lax.all_to_all(spread, ("hidden", "expert"), 0, 0, tiled=True)
    theirs = lax.ppermute(mine, "expert", perm=pairs)
    first = jnp.where(core == 0, mine, theirs)
    second = jnp.where(core == 0, theirs, mine)
    full = jnp.concatenate([first, second], axis=1).reshape(hid, exp, tok_rows, width)

    routing = full[:, 0, :, feat : feat + 4 * top].astype(jnp.float32).reshape(hid * tok_rows, 4 * top)
    ids = routing[:, :top]
    gates = routing[:, top : 2 * top] + routing[:, 2 * top : 3 * top] + routing[:, 3 * top : 4 * top]
    weight = jnp.sum(jnp.where(ids == me.astype(jnp.float32), gates, 0.0), axis=1)

    slabs = full.transpose(1, 0, 2, 3).reshape(exp, hid * tok_rows, width)
    partial = expert_ffn(slabs, w_gate[0], w_up[0], w_down[0])
    weighted = (partial * weight[:, None]).reshape(hid, 2, half, exp * feat)

    keep = jnp.where(core == 0, weighted[:, 0], weighted[:, 1])
    give = jnp.where(core == 0, weighted[:, 1], weighted[:, 0])
    chip_sum = keep + lax.ppermute(give, "expert", perm=pairs)

    outgoing = (
        chip_sum.astype(jnp.bfloat16)
        .reshape(hid, half, exp, feat)
        .transpose(0, 2, 1, 3)
        .reshape(groups, half, feat)
    )
    incoming = lax.all_to_all(outgoing, ("hidden", "expert"), 0, 0, tiled=True)
    incoming = incoming.reshape(hid, exp // 2, 2, half, feat).astype(jnp.float32)
    mixed = jnp.sum(incoming, axis=(0, 1)).reshape(tok_rows, feat)
    return mixed.astype(jnp.bfloat16)


def solution(mesh):
    placed = (
        P("hidden", "expert"),
        P("hidden", None),
        P("hidden", None),
        P("expert", None, "hidden"),
        P("expert", None, "hidden"),
        P("expert", "hidden", None),
    )
    return jax.shard_map(
        per_device, mesh=mesh, in_specs=placed, out_specs=P("hidden", "expert"), check_vma=False
    )
```

```python
import jax
import jax.numpy as jnp
from jax import lax
from jax.sharding import PartitionSpec as P

LANE = 128


def per_device(tokens, expert_ids, gate_vals, w_gate, w_up, w_down):
    hid = lax.axis_size("hidden")
    exp = lax.axis_size("expert")
    tok_rows, feat = tokens.shape
    top = expert_ids.shape[1]
    groups = hid * exp
    half = tok_rows // 2
    me = lax.axis_index("expert")
    core = me % 2
    pairs = [(i, i ^ 1) for i in range(exp)]

    ids_f = expert_ids.astype(jnp.float32)
    cols = jnp.concatenate([ids_f, gate_vals, gate_vals, gate_vals], axis=1)
    hi = lax.reduce_precision(cols, exponent_bits=8, mantissa_bits=7)
    mid = lax.reduce_precision(cols - hi, exponent_bits=8, mantissa_bits=7)
    lo = cols - hi - mid
    group = lax.broadcasted_iota(jnp.int32, cols.shape, 1) // top
    route = jnp.where(group == 0, cols, jnp.where(group == 1, hi, jnp.where(group == 2, mid, lo)))
    route = jnp.pad(route, ((0, 0), (0, LANE - route.shape[1])))
    wide = jnp.concatenate([tokens, route.astype(jnp.bfloat16)], axis=1)
    width = wide.shape[1]

    halves = wide.reshape(1, 1, 2, half, width)
    spread = jnp.broadcast_to(halves, (hid, exp // 2, 2, half, width)).reshape(groups, half, width)
    mine = lax.all_to_all(spread, ("hidden", "expert"), 0, 0, tiled=True)
    theirs = lax.ppermute(mine, "expert", perm=pairs)
    first = jnp.where(core == 0, mine, theirs)
    second = jnp.where(core == 0, theirs, mine)
    full = jnp.concatenate([first, second], axis=1).reshape(hid, exp, tok_rows, width)

    token_pieces = full[..., :feat]
    routing = full[:, 0, :, feat : feat + 4 * top].astype(jnp.float32).reshape(hid * tok_rows, 4 * top)
    ids = routing[:, :top]
    gates = routing[:, top : 2 * top] + routing[:, 2 * top : 3 * top] + routing[:, 3 * top : 4 * top]
    weight = jnp.sum(jnp.where(ids == me.astype(jnp.float32), gates, 0.0), axis=1)

    ff = w_gate.shape[2]

    def project(weights):
        blocks = weights[0].reshape(exp, feat, ff)
        out = jnp.einsum("herf,efn->hrn", token_pieces, blocks, preferred_element_type=jnp.float32)
        return out.reshape(hid * tok_rows, ff)

    gate_part = project(w_gate)
    up_part = project(w_up)
    hidden = lax.optimization_barrier((jax.nn.silu(gate_part) * up_part).astype(jnp.bfloat16))
    partial = jnp.dot(hidden, w_down[0], preferred_element_type=jnp.float32)
    weighted = (partial * weight[:, None]).reshape(hid, 2, half, exp * feat)

    keep = jnp.where(core == 0, weighted[:, 0], weighted[:, 1])
    give = jnp.where(core == 0, weighted[:, 1], weighted[:, 0])
    chip_sum = keep + lax.ppermute(give.astype(jnp.bfloat16), "expert", perm=pairs).astype(jnp.float32)

    outgoing = (
        chip_sum.astype(jnp.bfloat16)
        .reshape(hid, half, exp, feat)
        .transpose(0, 2, 1, 3)
        .reshape(groups, half, feat)
    )
    incoming = lax.all_to_all(outgoing, ("hidden", "expert"), 0, 0, tiled=True)
    incoming = incoming.reshape(hid, exp // 2, 2, half, feat).astype(jnp.float32)
    mixed = jnp.sum(incoming, axis=(0, 1)).reshape(tok_rows, feat)
    return mixed.astype(jnp.bfloat16)


def solution(mesh):
    placed = (
        P("hidden", "expert"),
        P("hidden", None),
        P("hidden", None),
        P("expert", None, "hidden"),
        P("expert", None, "hidden"),
        P("expert", "hidden", None),
    )
    return jax.shard_map(
        per_device, mesh=mesh, in_specs=placed, out_specs=P("hidden", "expert"), check_vma=False
    )
```

```python
import jax
import jax.numpy as jnp
from jax import lax
from jax.sharding import PartitionSpec as P

LANE = 128


def per_device(tokens, expert_ids, gate_vals, w_gate, w_up, w_down):
    hid = lax.axis_size("hidden")
    exp = lax.axis_size("expert")
    tok_rows, feat = tokens.shape
    top = expert_ids.shape[1]
    groups = hid * exp
    half = tok_rows // 2
    me = lax.axis_index("expert")
    core = me % 2
    pairs = [(i, i ^ 1) for i in range(exp)]

    ids_f = expert_ids.astype(jnp.float32)
    cols = jnp.concatenate([ids_f, gate_vals, gate_vals, gate_vals], axis=1)
    hi = lax.reduce_precision(cols, exponent_bits=8, mantissa_bits=7)
    mid = lax.reduce_precision(cols - hi, exponent_bits=8, mantissa_bits=7)
    lo = cols - hi - mid
    group = lax.broadcasted_iota(jnp.int32, cols.shape, 1) // top
    route = jnp.where(group == 0, cols, jnp.where(group == 1, hi, jnp.where(group == 2, mid, lo)))
    route = jnp.pad(route, ((0, 0), (0, LANE - route.shape[1])))
    wide = jnp.concatenate([tokens, route.astype(jnp.bfloat16)], axis=1)
    width = wide.shape[1]

    halves = wide.reshape(1, 1, 2, half, width)
    spread = jnp.broadcast_to(halves, (hid, exp // 2, 2, half, width)).reshape(groups, half, width)
    mine = lax.all_to_all(spread, ("hidden", "expert"), 0, 0, tiled=True)
    theirs = lax.ppermute(mine, "expert", perm=pairs)
    first = jnp.where(core == 0, mine, theirs)
    second = jnp.where(core == 0, theirs, mine)
    full = jnp.concatenate([first, second], axis=1).reshape(hid, exp, tok_rows, width)

    token_pieces = full[..., :feat]
    routing = full[:, 0, :, feat : feat + 4 * top].astype(jnp.float32).reshape(hid * tok_rows, 4 * top)
    ids = routing[:, :top]
    gates = routing[:, top : 2 * top] + routing[:, 2 * top : 3 * top] + routing[:, 3 * top : 4 * top]
    weight = jnp.sum(jnp.where(ids == me.astype(jnp.float32), gates, 0.0), axis=1)

    ff = w_gate.shape[2]

    def project(weights):
        blocks = weights[0].reshape(exp, feat, ff)
        cut = ff // 2
        outs = [
            jnp.einsum("herf,efn->hrn", token_pieces, blocks[..., :cut], preferred_element_type=jnp.float32),
            jnp.einsum("herf,efn->hrn", token_pieces, blocks[..., cut:], preferred_element_type=jnp.float32),
        ]
        return jnp.concatenate(outs, axis=-1).reshape(hid * tok_rows, ff)

    gate_part = project(w_gate)
    up_part = project(w_up)
    hidden = lax.optimization_barrier((jax.nn.silu(gate_part) * up_part).astype(jnp.bfloat16))
    partial = jnp.dot(hidden, w_down[0], preferred_element_type=jnp.float32)
    weighted = (partial * weight[:, None]).reshape(hid, 2, half, exp * feat)

    keep = jnp.where(core == 0, weighted[:, 0], weighted[:, 1])
    give = jnp.where(core == 0, weighted[:, 1], weighted[:, 0])
    chip_sum = keep + lax.ppermute(give.astype(jnp.bfloat16), "expert", perm=pairs).astype(jnp.float32)

    outgoing = (
        chip_sum.astype(jnp.bfloat16)
        .reshape(hid, half, exp, feat)
        .transpose(0, 2, 1, 3)
        .reshape(groups, half, feat)
    )
    incoming = lax.all_to_all(outgoing, ("hidden", "expert"), 0, 0, tiled=True)
    incoming = incoming.reshape(hid, exp // 2, 2, half, feat).astype(jnp.float32)
    mixed = jnp.sum(incoming, axis=(0, 1)).reshape(tok_rows, feat)
    return mixed.astype(jnp.bfloat16)


def solution(mesh):
    placed = (
        P("hidden", "expert"),
        P("hidden", None),
        P("hidden", None),
        P("expert", None, "hidden"),
        P("expert", None, "hidden"),
        P("expert", "hidden", None),
    )
    return jax.shard_map(
        per_device, mesh=mesh, in_specs=placed, out_specs=P("hidden", "expert"), check_vma=False
    )
```

```python
import jax
import jax.numpy as jnp
from jax import lax
from jax.sharding import PartitionSpec as P

LANE = 128


def per_device(tokens, expert_ids, gate_vals, w_gate, w_up, w_down):
    hid = lax.axis_size("hidden")
    exp = lax.axis_size("expert")
    tok_rows, feat = tokens.shape
    top = expert_ids.shape[1]
    groups = hid * exp
    half = tok_rows // 2
    me = lax.axis_index("expert")
    core = me % 2
    pairs = [(i, i ^ 1) for i in range(exp)]

    ids_f = expert_ids.astype(jnp.float32)
    cols = jnp.concatenate([ids_f, gate_vals, gate_vals, gate_vals], axis=1)
    hi = lax.reduce_precision(cols, exponent_bits=8, mantissa_bits=7)
    mid = lax.reduce_precision(cols - hi, exponent_bits=8, mantissa_bits=7)
    lo = cols - hi - mid
    group = lax.broadcasted_iota(jnp.int32, cols.shape, 1) // top
    route = jnp.where(group == 0, cols, jnp.where(group == 1, hi, jnp.where(group == 2, mid, lo)))
    route = jnp.pad(route, ((0, 0), (0, LANE - route.shape[1])))
    wide = jnp.concatenate([tokens, route.astype(jnp.bfloat16)], axis=1)
    width = wide.shape[1]

    halves = wide.reshape(1, 1, 2, half, width)
    spread = jnp.broadcast_to(halves, (hid, exp // 2, 2, half, width)).reshape(groups, half, width)
    mine = lax.all_to_all(spread, ("hidden", "expert"), 0, 0, tiled=True)
    theirs = lax.ppermute(mine, "expert", perm=pairs)
    first = jnp.where(core == 0, mine, theirs)
    second = jnp.where(core == 0, theirs, mine)
    full = jnp.concatenate([first, second], axis=1).reshape(hid, exp, tok_rows, width)

    token_pieces = full[..., :feat]
    routing = full[:, 0, :, feat : feat + 4 * top].astype(jnp.float32).reshape(hid * tok_rows, 4 * top)
    ids = routing[:, :top]
    gates = routing[:, top : 2 * top] + routing[:, 2 * top : 3 * top] + routing[:, 3 * top : 4 * top]
    weight = jnp.sum(jnp.where(ids == me.astype(jnp.float32), gates, 0.0), axis=1)

    ff = w_gate.shape[2]

    def project(weights):
        blocks = weights[0].reshape(exp, feat, ff)
        out = jnp.einsum("herf,efn->hrn", token_pieces, blocks, preferred_element_type=jnp.float32)
        return out.reshape(hid * tok_rows, ff)

    gate_w = w_gate[0].reshape(exp, feat, ff)
    own = mine.reshape(hid, exp, half, width)[..., :feat]
    other = theirs.reshape(hid, exp, half, width)[..., :feat]
    gate_own = jnp.einsum("herf,efn->hrn", own, gate_w, preferred_element_type=jnp.float32)
    gate_other = jnp.einsum("herf,efn->hrn", other, gate_w, preferred_element_type=jnp.float32)
    gate_part = jnp.concatenate(
        [jnp.where(core == 0, gate_own, gate_other), jnp.where(core == 0, gate_other, gate_own)], axis=1
    ).reshape(hid * tok_rows, ff)
    up_part = project(w_up)
    hidden = lax.optimization_barrier((jax.nn.silu(gate_part) * up_part).astype(jnp.bfloat16))
    partial = jnp.dot(hidden, w_down[0], preferred_element_type=jnp.float32)
    weighted = (partial * weight[:, None]).reshape(hid, 2, half, exp * feat)

    keep = jnp.where(core == 0, weighted[:, 0], weighted[:, 1])
    give = jnp.where(core == 0, weighted[:, 1], weighted[:, 0])
    chip_sum = keep + lax.ppermute(give.astype(jnp.bfloat16), "expert", perm=pairs).astype(jnp.float32)

    outgoing = (
        chip_sum.astype(jnp.bfloat16)
        .reshape(hid, half, exp, feat)
        .transpose(0, 2, 1, 3)
        .reshape(groups, half, feat)
    )
    incoming = lax.all_to_all(outgoing, ("hidden", "expert"), 0, 0, tiled=True)
    incoming = incoming.reshape(hid, exp // 2, 2, half, feat).astype(jnp.float32)
    mixed = jnp.sum(incoming, axis=(0, 1)).reshape(tok_rows, feat)
    return mixed.astype(jnp.bfloat16)


def solution(mesh):
    placed = (
        P("hidden", "expert"),
        P("hidden", None),
        P("hidden", None),
        P("expert", None, "hidden"),
        P("expert", None, "hidden"),
        P("expert", "hidden", None),
    )
    return jax.shard_map(
        per_device, mesh=mesh, in_specs=placed, out_specs=P("hidden", "expert"), check_vma=False
    )
```

```python
import jax
import jax.numpy as jnp
from jax import lax
from jax.sharding import PartitionSpec as P

LANE = 128


def per_device(tokens, expert_ids, gate_vals, w_gate, w_up, w_down):
    hid = lax.axis_size("hidden")
    exp = lax.axis_size("expert")
    tok_rows, feat = tokens.shape
    top = expert_ids.shape[1]
    groups = hid * exp
    half = tok_rows // 2
    me = lax.axis_index("expert")
    core = me % 2
    pairs = [(i, i ^ 1) for i in range(exp)]

    ids_t = expert_ids.T.astype(jnp.float32)
    gates_t = gate_vals.T
    hi = lax.reduce_precision(gates_t, exponent_bits=8, mantissa_bits=7)
    mid = lax.reduce_precision(gates_t - hi, exponent_bits=8, mantissa_bits=7)
    lo = gates_t - hi - mid
    route = jnp.concatenate([ids_t, hi, mid, lo], axis=0).T
    route = jnp.pad(route, ((0, 0), (0, LANE - route.shape[1])))
    wide = jnp.concatenate([tokens, route.astype(jnp.bfloat16)], axis=1)
    width = wide.shape[1]

    halves = wide.reshape(1, 1, 2, half, width)
    spread = jnp.broadcast_to(halves, (hid, exp // 2, 2, half, width)).reshape(groups, half, width)
    mine = lax.all_to_all(spread, ("hidden", "expert"), 0, 0, tiled=True)
    theirs = lax.ppermute(mine, "expert", perm=pairs)
    first = jnp.where(core == 0, mine, theirs)
    second = jnp.where(core == 0, theirs, mine)
    full = jnp.concatenate([first, second], axis=1).reshape(hid, exp, tok_rows, width)

    token_pieces = full[..., :feat]
    routing = full[:, 0, :, feat : feat + 4 * top].astype(jnp.float32).reshape(hid * tok_rows, 4 * top)
    ids = routing[:, :top]
    gates = routing[:, top : 2 * top] + routing[:, 2 * top : 3 * top] + routing[:, 3 * top : 4 * top]
    weight = jnp.sum(jnp.where(ids == me.astype(jnp.float32), gates, 0.0), axis=1)

    ff = w_gate.shape[2]

    def project(weights):
        blocks = weights[0].reshape(exp, feat, ff)
        out = jnp.einsum("herf,efn->hrn", token_pieces, blocks, preferred_element_type=jnp.float32)
        return out.reshape(hid * tok_rows, ff)

    gate_part = project(w_gate)
    up_part = project(w_up)
    hidden = lax.optimization_barrier((jax.nn.silu(gate_part) * up_part).astype(jnp.bfloat16))
    partial = jnp.dot(hidden, w_down[0], preferred_element_type=jnp.float32)
    weighted = (partial * weight[:, None]).reshape(hid, 2, half, exp * feat)

    keep = jnp.where(core == 0, weighted[:, 0], weighted[:, 1])
    give = jnp.where(core == 0, weighted[:, 1], weighted[:, 0])
    chip_sum = keep + lax.ppermute(give.astype(jnp.bfloat16), "expert", perm=pairs).astype(jnp.float32)

    outgoing = (
        chip_sum.astype(jnp.bfloat16)
        .reshape(hid, half, exp, feat)
        .transpose(0, 2, 1, 3)
        .reshape(groups, half, feat)
    )
    incoming = lax.all_to_all(outgoing, ("hidden", "expert"), 0, 0, tiled=True)
    incoming = incoming.reshape(hid, exp // 2, 2, half, feat).astype(jnp.float32)
    mixed = jnp.sum(incoming, axis=(0, 1)).reshape(tok_rows, feat)
    return mixed.astype(jnp.bfloat16)


def solution(mesh):
    placed = (
        P("hidden", "expert"),
        P("hidden", None),
        P("hidden", None),
        P("expert", None, "hidden"),
        P("expert", None, "hidden"),
        P("expert", "hidden", None),
    )
    return jax.shard_map(
        per_device, mesh=mesh, in_specs=placed, out_specs=P("hidden", "expert"), check_vma=False
    )
```

```python
import jax
import jax.numpy as jnp
from jax import lax
from jax.sharding import PartitionSpec as P

LANE = 128


def per_device(tokens, expert_ids, gate_vals, w_gate, w_up, w_down):
    hid = lax.axis_size("hidden")
    exp = lax.axis_size("expert")
    tok_rows, feat = tokens.shape
    top = expert_ids.shape[1]
    groups = hid * exp
    half = tok_rows // 2
    me = lax.axis_index("expert")
    core = me % 2
    pairs = [(i, i ^ 1) for i in range(exp)]

    ids_t = expert_ids.T.astype(jnp.float32)
    gates_t = gate_vals.T
    hi = lax.reduce_precision(gates_t, exponent_bits=8, mantissa_bits=7)
    mid = lax.reduce_precision(gates_t - hi, exponent_bits=8, mantissa_bits=7)
    lo = gates_t - hi - mid
    route = jnp.concatenate([ids_t, hi, mid, lo], axis=0).T
    route = jnp.pad(route, ((0, 0), (0, LANE - route.shape[1])))
    wide = jnp.concatenate([tokens, route.astype(jnp.bfloat16)], axis=1)
    width = wide.shape[1]

    halves = wide.reshape(1, 2, 1, half, width)
    spread = jnp.broadcast_to(halves, (exp // 2, 2, hid, half, width)).reshape(groups, half, width)
    mine = lax.all_to_all(spread, ("expert", "hidden"), 0, 0, tiled=True)
    mine = mine.reshape(exp, hid, half, width).transpose(1, 0, 2, 3).reshape(groups, half, width)
    theirs = lax.ppermute(mine, "expert", perm=pairs)
    first = jnp.where(core == 0, mine, theirs)
    second = jnp.where(core == 0, theirs, mine)
    full = jnp.concatenate([first, second], axis=1).reshape(hid, exp, tok_rows, width)

    token_pieces = full[..., :feat]
    routing = full[:, 0, :, feat : feat + 4 * top].astype(jnp.float32).reshape(hid * tok_rows, 4 * top)
    ids = routing[:, :top]
    gates = routing[:, top : 2 * top] + routing[:, 2 * top : 3 * top] + routing[:, 3 * top : 4 * top]
    weight = jnp.sum(jnp.where(ids == me.astype(jnp.float32), gates, 0.0), axis=1)

    ff = w_gate.shape[2]

    def project(weights):
        blocks = weights[0].reshape(exp, feat, ff)
        out = jnp.einsum("herf,efn->hrn", token_pieces, blocks, preferred_element_type=jnp.float32)
        return out.reshape(hid * tok_rows, ff)

    gate_part = project(w_gate)
    up_part = project(w_up)
    hidden = lax.optimization_barrier((jax.nn.silu(gate_part) * up_part).astype(jnp.bfloat16))
    partial = jnp.dot(hidden, w_down[0], preferred_element_type=jnp.float32)
    weighted = (partial * weight[:, None]).reshape(hid, 2, half, exp * feat)

    keep = jnp.where(core == 0, weighted[:, 0], weighted[:, 1])
    give = jnp.where(core == 0, weighted[:, 1], weighted[:, 0])
    chip_sum = keep + lax.ppermute(give.astype(jnp.bfloat16), "expert", perm=pairs).astype(jnp.float32)

    outgoing = (
        chip_sum.astype(jnp.bfloat16)
        .reshape(hid, half, exp, feat)
        .transpose(2, 0, 1, 3)
        .reshape(groups, half, feat)
    )
    incoming = lax.all_to_all(outgoing, ("expert", "hidden"), 0, 0, tiled=True)
    incoming = incoming.reshape(exp // 2, 2, hid, half, feat).astype(jnp.float32)
    mixed = jnp.sum(incoming, axis=(0, 2)).reshape(tok_rows, feat)
    return mixed.astype(jnp.bfloat16)


def solution(mesh):
    placed = (
        P("hidden", "expert"),
        P("hidden", None),
        P("hidden", None),
        P("expert", None, "hidden"),
        P("expert", None, "hidden"),
        P("expert", "hidden", None),
    )
    return jax.shard_map(
        per_device, mesh=mesh, in_specs=placed, out_specs=P("hidden", "expert"), check_vma=False
    )
```
